256 devices in a mesh: dp: 32 (over x, z), mp: 8 (over y, core).
Axes of the slice: x: 4, y: 4, z: 8, core: 2. Of those that a mesh axis runs over, the one named last changes fastest.
Arguments:
- tokens: bfloat16 [8192, 8192], P(('dp', 'mp')), may hold values from -6 to 6
- upstream: bfloat16 [8192, 2, 28672], P(('dp', 'mp')), may hold values from -0.0625 to 0.0625
- deltas: bfloat16 [1024, 128, 128], P('mp'), may hold values from -0.5 to 0.5
- block_row: int32 [1024], P('mp'), may hold values from 0 to 63, as said below
- block_column: int32 [1024], P('mp'), may hold values from 0 to 55, as said below
- block_owner: int32 [1024], P('mp'), may hold values from 0 to 31, as said below
- block_count: int32 [8], P('mp'), may hold values from 64 to 128, as said below
Outputs:
- branch_out: bfloat16 [8192, 2, 28672], P('dp', None, 'mp')
- block_grads: float32 [8, 192, 128, 128], P('mp', 'dp')
The draws below stay inside these ranges and needn't reach their ends.
Inputs may be any that keep to these rules, and one draw needn't show every extreme that they name: `block_row`: row tile of each slot's delta tile. `block_column`: column tile within the shard's gate columns (below 28) followed by its up columns; the tiles of one shard's slots are distinct. `block_owner`: among the live slots of one shard no dp index owns more than 6 tiles, and in every shard one dp index owns exactly 6. The live slots of a shard are its first block_count slots; some shard has all 128 live.
All inputs are finite; a program needn't handle non-finite values.
Results may differ from the reference program's by a relative error of at most 0.001.
Values may be sent and summed in bfloat16 or wider, within the bound.
No kernel may reach another device: no remote copies, remote signals or barrier semaphores. Data moves between devices by JAX's collectives and lax.ppermute only.
A program may use at most 128 MiB of HBM per device.

```python
import jax
import jax.numpy as jnp
from jax import lax

D = 8192
FF = 28672
BLK = 128
CAP = 128
OCAP = 6
TOKENS = 8192
N_DP = 32
N_MP = 8


def layout_draw(key):
    base_key = jax.random.fold_in(key, 4242)
    row_blocks = D // BLK
    column_blocks = 2 * FF // (BLK * N_MP)
    half_cap = CAP // 2
    slot_ids = jnp.arange(CAP, dtype=jnp.int32)

    def one_shard(shard_key):
        perm_key, owner_key, shuffle_key = jax.random.split(shard_key, 3)
        positions = jax.random.permutation(perm_key, row_blocks * column_blocks)[:CAP].astype(jnp.int32)
        owner_order = jax.random.permutation(owner_key, N_DP).astype(jnp.int32)
        cyclic = owner_order[1 + (slot_ids - OCAP) % (N_DP - 1)]
        owners = jnp.where(slot_ids < OCAP, owner_order[0], cyclic)
        mixing = jax.random.permutation(shuffle_key, half_cap)
        owners = jnp.concatenate([owners[:half_cap][mixing], owners[half_cap:]])
        return (positions // column_blocks, positions % column_blocks, owners)
    row_ids, column_ids, owners = jax.vmap(one_shard)(jax.random.split(base_key, N_MP))
    count_key, full_key = jax.random.split(jax.random.fold_in(base_key, 99))
    counts = jax.random.randint(count_key, (N_MP,), CAP // 2, CAP + 1, dtype=jnp.int32)
    full_shard = jax.random.randint(full_key, (), 0, N_MP, dtype=jnp.int32)
    counts = jnp.where(jnp.arange(N_MP, dtype=jnp.int32) == full_shard, CAP, counts)
    return (row_ids.reshape(-1).astype(jnp.int32), column_ids.reshape(-1).astype(jnp.int32), owners.reshape(-1).astype(jnp.int32), counts.astype(jnp.int32))


def draw_block_row(key, part):
    return layout_draw(key)[0]


def draw_block_column(key, part):
    return layout_draw(key)[1]


def draw_block_owner(key, part):
    return layout_draw(key)[2]


def draw_block_count(key, part):
    return layout_draw(key)[3]


def shard_levels(stream_key, extent, shards, least, high):
    def one(position, parts):
        steps = jax.random.uniform(jax.random.fold_in(jax.random.fold_in(stream_key, 6), position), (parts,), jnp.float32, least / len(shards), high / len(shards))
        return jnp.repeat(jnp.exp(steps), extent[position] // parts).reshape((-1,) + (1,) * (len(extent) - position - 1))

    factor_of = one(*shards[0])
    for cut in shards[1:]:
        factor_of = factor_of * one(*cut)
    return factor_of


def bell_draw(key, shape, scale, bound, cuts=(), kind=jnp.bfloat16):
    loudness = shard_levels(key, shape, cuts, -0.22, 0.18) if cuts else 1.0
    result = jax.random.normal(key, shape, jnp.float32) * scale * loudness
    return jnp.minimum(jnp.maximum(result, -bound), bound).astype(kind)


def setup_inputs(seed: int = 0) -> dict:
    key_of = jax.random.split(jax.random.key(seed), 8)
    tokens = bell_draw(key_of[0], (TOKENS, D), 1.0, 6.0, ((0, 256),))
    upstream = bell_draw(key_of[1], (TOKENS, 2, FF), TOKENS ** -0.5, 0.0625, ((0, 256),))
    deltas = bell_draw(key_of[2], (N_MP * CAP, BLK, BLK), BLK ** -0.5, 0.5, ((0, 8),))
    block_row = draw_block_row(jax.random.fold_in(key_of[7], 71), 0)
    block_column = draw_block_column(jax.random.fold_in(key_of[7], 71), 0)
    block_owner = draw_block_owner(jax.random.fold_in(key_of[7], 71), 0)
    block_count = draw_block_count(jax.random.fold_in(key_of[7], 71), 0)
    return {"tokens": tokens, "upstream": upstream, "deltas": deltas, "block_row": block_row, "block_column": block_column, "block_owner": block_owner, "block_count": block_count}


def owner_ranks(owners, live_slots, dp_count):
    owner_hot = ((owners[:, None] == jnp.arange(dp_count, dtype=jnp.int32)[None, :]) & live_slots[:, None]).astype(jnp.int32)
    before = jnp.cumsum(owner_hot, axis=0) - owner_hot
    return jnp.sum(before * owner_hot, axis=1).astype(jnp.int32)


def pick_tiles(source, chosen):
    slot_ids = jnp.arange(chosen.shape[1], dtype=jnp.int32)
    source_index = jnp.sum(jnp.where(chosen, slot_ids[None, :], 0), axis=1).astype(jnp.int32)
    present = jnp.any(chosen, axis=1).astype(jnp.float32)
    return jnp.take(source, source_index, axis=0) * present[:, None, None]


def reference(tokens, upstream, deltas, block_row, block_column, block_owner, block_count):
    token_total = tokens.shape[0]
    shard_width = FF // N_MP
    column_blocks = 2 * shard_width // BLK
    row_tiles = tokens.reshape(token_total, D // BLK, BLK)
    slot_ids = jnp.arange(CAP, dtype=jnp.int32)
    owner_slots = jnp.arange(N_DP * OCAP, dtype=jnp.int32)
    column_ids = jnp.arange(column_blocks, dtype=jnp.int32)

    def per_shard(shard_index):
        first_slot = (shard_index * CAP).astype(jnp.int32)
        rows_here = lax.dynamic_slice_in_dim(block_row, first_slot, CAP)
        columns_here = lax.dynamic_slice_in_dim(block_column, first_slot, CAP)
        owners_here = lax.dynamic_slice_in_dim(block_owner, first_slot, CAP)
        delta_tiles = lax.dynamic_slice_in_dim(deltas, first_slot, CAP, 0).astype(jnp.float32)
        live_slots = slot_ids < block_count[shard_index]
        column_part = lax.dynamic_slice_in_dim(upstream, (shard_index * shard_width).astype(jnp.int32), shard_width, 2)
        column_tiles = column_part.reshape(token_total, column_blocks, BLK)
        feature_tiles = jnp.take(row_tiles, rows_here, axis=1).astype(jnp.float32)
        upstream_tiles = jnp.take(column_tiles, columns_here, axis=1).astype(jnp.float32)
        product = jnp.einsum("tki,kio->tko", feature_tiles, delta_tiles, precision=lax.Precision.HIGHEST)
        column_table = (live_slots[:, None] & (columns_here[:, None] == column_ids[None, :])).astype(jnp.float32)
        placed = jnp.einsum("tko,kc->tco", product, column_table, precision=lax.Precision.HIGHEST)
        branch = placed.reshape(token_total, 2, shard_width).astype(jnp.bfloat16)
        tile_grad = jnp.einsum("tki,tko->kio", feature_tiles, upstream_tiles, precision=lax.Precision.HIGHEST)
        owner_rank = owner_ranks(owners_here, live_slots, N_DP)
        targets = owners_here * OCAP + owner_rank
        chosen = live_slots[None, :] & (targets[None, :] == owner_slots[:, None])
        return branch, pick_tiles(tile_grad, chosen)

    branches, block_grads = lax.map(per_shard, jnp.arange(N_MP, dtype=jnp.int32))
    branch_out = jnp.transpose(branches, (1, 2, 0, 3)).reshape(token_total, 2, FF)
    return branch_out, block_grads
```

```python
import jax
import jax.numpy as jnp
from jax import lax
from jax.sharding import PartitionSpec as P


def owner_slots(block_owner, live_slots, dp_count, owner_cap):
    owner_hot = (
        (block_owner[:, None] == jnp.arange(dp_count, dtype=jnp.int32)[None, :])
        & live_slots[:, None]
    ).astype(jnp.int32)
    before = jnp.cumsum(owner_hot, axis=0) - owner_hot
    owner_rank = jnp.sum(before * owner_hot, axis=1)
    targets = block_owner * owner_cap + owner_rank
    slot_ids = jnp.arange(dp_count * owner_cap, dtype=jnp.int32)
    chosen = live_slots[None, :] & (targets[None, :] == slot_ids[:, None])
    entry_ids = jnp.arange(block_owner.shape[0], dtype=jnp.int32)
    source_index = jnp.sum(jnp.where(chosen, entry_ids[None, :], 0), axis=1).astype(jnp.int32)
    present = jnp.any(chosen, axis=1)
    return source_index, present


def gather_columns(upstream, mp_count):
    me = lax.axis_index("mp")
    width = upstream.shape[2] // mp_count
    pieces = [None] * mp_count
    for shift in range(mp_count):
        target = (me + shift) % mp_count
        piece = lax.dynamic_slice_in_dim(upstream, target * width, width, 2)
        if shift:
            perm = [(m, (m + shift) % mp_count) for m in range(mp_count)]
            piece = lax.ppermute(piece, "mp", perm)
        pieces[shift] = piece
    stacked = jnp.stack(pieces, axis=0)
    shift_of_source = (me - jnp.arange(mp_count, dtype=jnp.int32)) % mp_count
    ordered = jnp.take(stacked, shift_of_source, axis=0)
    return ordered.reshape((mp_count * upstream.shape[0],) + upstream.shape[1:2] + (width,))


def local(tokens, upstream, deltas, block_row, block_column, block_owner, block_count):
    model_width = tokens.shape[1]
    tile_size = deltas.shape[1]
    slot_count = deltas.shape[0]
    mp_count = lax.axis_size("mp")
    dp_count = lax.axis_size("dp")
    hidden = gather_columns(upstream, mp_count)
    group_rows = hidden.shape[0]
    column_blocks = hidden.shape[1] * hidden.shape[2] // tile_size
    hidden_major = jnp.transpose(hidden.reshape(group_rows, column_blocks, tile_size), (1, 0, 2))
    upstream_chosen = jnp.take(hidden_major, block_column, axis=0)
    slot_ids = jnp.arange(slot_count, dtype=jnp.int32)
    live_slots = slot_ids < block_count[0]
    column_table = (
        live_slots[:, None]
        & (block_column[:, None] == jnp.arange(column_blocks, dtype=jnp.int32)[None, :])
    ).astype(jnp.float32)
    shard_rows = lax.all_gather(tokens, "mp", axis=0, tiled=True)
    row_count = shard_rows.shape[0]
    row_major = jnp.transpose(
        shard_rows.reshape(row_count, model_width // tile_size, tile_size), (1, 0, 2)
    )
    feature_tiles = jnp.take(row_major, block_row, axis=0)
    grad_sum = jnp.einsum(
        "kni,kno->kio", feature_tiles, upstream_chosen, preferred_element_type=jnp.float32
    )
    owner_cap = 3 * slot_count // (2 * dp_count)
    source_index, present = owner_slots(block_owner, live_slots, dp_count, owner_cap)
    by_slot = jnp.where(present[:, None, None], jnp.take(grad_sum, source_index, axis=0), 0.0)
    owned = lax.psum_scatter(by_slot, "dp", scatter_dimension=0, tiled=True)
    product = jnp.einsum("kni,kio->kno", feature_tiles, deltas, preferred_element_type=jnp.float32)
    rows_out = jnp.einsum("kc,kno->cno", column_table, product, precision=lax.Precision.HIGHEST)
    branch_out = jnp.transpose(rows_out.astype(jnp.bfloat16), (1, 0, 2)).reshape(
        group_rows, hidden.shape[1], hidden.shape[2]
    )
    return (branch_out, owned[None])


def solution(mesh):
    placed = (
        P(("dp", "mp"), None),
        P(("dp", "mp"), None, None),
        P("mp", None, None),
        P("mp"),
        P("mp"),
        P("mp"),
        P("mp"),
    )
    return jax.shard_map(
        local,
        mesh=mesh,
        in_specs=placed,
        out_specs=(P("dp", None, "mp"), P("mp", "dp", None, None)),
        check_vma=False,
    )
```

```python
import jax
import jax.numpy as jnp
from jax import lax
from jax.sharding import PartitionSpec as P


def owner_slots(block_owner, live_slots, dp_count, owner_cap, row_len):
    owner_hot = (
        (block_owner[:, None] == jnp.arange(dp_count, dtype=jnp.int32)[None, :])
        & live_slots[:, None]
    ).astype(jnp.int32)
    before = jnp.cumsum(owner_hot, axis=0) - owner_hot
    owner_rank = jnp.sum(before * owner_hot, axis=1)
    x_count = dp_count // row_len
    owner_x = block_owner // row_len
    owner_z = block_owner % row_len
    targets = owner_z * (x_count * owner_cap) + owner_x * owner_cap + owner_rank
    slot_ids = jnp.arange(dp_count * owner_cap, dtype=jnp.int32)
    chosen = live_slots[None, :] & (targets[None, :] == slot_ids[:, None])
    entry_ids = jnp.arange(block_owner.shape[0], dtype=jnp.int32)
    source_index = jnp.sum(jnp.where(chosen, entry_ids[None, :], 0), axis=1).astype(jnp.int32)
    present = jnp.any(chosen, axis=1)
    return source_index, present


def slot_tiles(grad_sum, source_index, present, start, count):
    index = lax.dynamic_slice_in_dim(source_index, start, count)
    keep = lax.dynamic_slice_in_dim(present, start, count)
    return jnp.where(keep[:, None, None], jnp.take(grad_sum, index, axis=0), 0.0)


def reduce_owned(grad_sum, source_index, present, dp_count, owner_cap, row_len):
    dp_me = lax.axis_index("dp")
    x_count = dp_count // row_len
    me_z = dp_me % row_len
    me_x = dp_me // row_len
    z_chunk = x_count * owner_cap
    z_half = z_chunk // 2
    x_half = owner_cap // 2

    def z_perm(shift):
        return [(i, (i // row_len) * row_len + (i % row_len + shift) % row_len) for i in range(dp_count)]

    def x_perm(shift):
        return [(i, (i + shift * row_len) % dp_count) for i in range(dp_count)]

    def z_part(c, h):
        return slot_tiles(grad_sum, source_index, present, c * z_chunk + h * z_half, z_half)

    cw = z_part((me_z - 1) % row_len, 0)
    ccw = z_part((me_z + 1) % row_len, 1)
    for k in range(row_len - 1):
        cw = lax.ppermute(cw, "dp", z_perm(1)) + z_part((me_z - k - 2) % row_len, 0)
        ccw = lax.ppermute(ccw, "dp", z_perm(-1)) + z_part((me_z + k + 2) % row_len, 1)
    row_sum = jnp.concatenate([cw, ccw], axis=0)

    def x_part(c, h):
        return lax.dynamic_slice_in_dim(row_sum, c * owner_cap + h * x_half, x_half, 0)

    cw = x_part((me_x - 1) % x_count, 0)
    ccw = x_part((me_x + 1) % x_count, 1)
    for k in range(x_count - 1):
        cw = lax.ppermute(cw, "dp", x_perm(1)) + x_part((me_x - k - 2) % x_count, 0)
        ccw = lax.ppermute(ccw, "dp", x_perm(-1)) + x_part((me_x + k + 2) % x_count, 1)
    return jnp.concatenate([cw, ccw], axis=0)


def gather_columns(upstream, mp_count):
    me = lax.axis_index("mp")
    width = upstream.shape[2] // mp_count
    pieces = [None] * mp_count
    for shift in range(mp_count):
        target = (me + shift) % mp_count
        piece = lax.dynamic_slice_in_dim(upstream, target * width, width, 2)
        if shift:
            perm = [(m, (m + shift) % mp_count) for m in range(mp_count)]
            piece = lax.ppermute(piece, "mp", perm)
        pieces[shift] = piece
    stacked = jnp.stack(pieces, axis=0)
    shift_of_source = (me - jnp.arange(mp_count, dtype=jnp.int32)) % mp_count
    ordered = jnp.take(stacked, shift_of_source, axis=0)
    return ordered.reshape((mp_count * upstream.shape[0],) + upstream.shape[1:2] + (width,))


def local(tokens, upstream, deltas, block_row, block_column, block_owner, block_count):
    model_width = tokens.shape[1]
    tile_size = deltas.shape[1]
    slot_count = deltas.shape[0]
    mp_count = lax.axis_size("mp")
    dp_count = lax.axis_size("dp")
    hidden = gather_columns(upstream, mp_count)
    group_rows = hidden.shape[0]
    column_blocks = hidden.shape[1] * hidden.shape[2] // tile_size
    hidden_major = jnp.transpose(hidden.reshape(group_rows, column_blocks, tile_size), (1, 0, 2))
    upstream_chosen = jnp.take(hidden_major, block_column, axis=0)
    slot_ids = jnp.arange(slot_count, dtype=jnp.int32)
    live_slots = slot_ids < block_count[0]
    column_table = (
        live_slots[:, None]
        & (block_column[:, None] == jnp.arange(column_blocks, dtype=jnp.int32)[None, :])
    ).astype(jnp.float32)
    shard_rows = lax.all_gather(tokens, "mp", axis=0, tiled=True)
    row_count = shard_rows.shape[0]
    row_major = jnp.transpose(
        shard_rows.reshape(row_count, model_width // tile_size, tile_size), (1, 0, 2)
    )
    feature_tiles = jnp.take(row_major, block_row, axis=0)
    grad_sum = jnp.einsum(
        "kni,kno->kio", feature_tiles, upstream_chosen, preferred_element_type=jnp.float32
    )
    owner_cap = 3 * slot_count // (2 * dp_count)
    row_len = 8 if dp_count % 8 == 0 else dp_count
    source_index, present = owner_slots(block_owner, live_slots, dp_count, owner_cap, row_len)
    owned = reduce_owned(grad_sum, source_index, present, dp_count, owner_cap, row_len)
    product = jnp.einsum("kni,kio->kno", feature_tiles, deltas, preferred_element_type=jnp.float32)
    rows_out = jnp.einsum("kc,kno->cno", column_table, product, precision=lax.Precision.HIGHEST)
    branch_out = jnp.transpose(rows_out.astype(jnp.bfloat16), (1, 0, 2)).reshape(
        group_rows, hidden.shape[1], hidden.shape[2]
    )
    return (branch_out, owned[None])


def solution(mesh):
    placed = (
        P(("dp", "mp"), None),
        P(("dp", "mp"), None, None),
        P("mp", None, None),
        P("mp"),
        P("mp"),
        P("mp"),
        P("mp"),
    )
    return jax.shard_map(
        local,
        mesh=mesh,
        in_specs=placed,
        out_specs=(P("dp", None, "mp"), P("mp", "dp", None, None)),
        check_vma=False,
    )
```

```python
import jax
import jax.numpy as jnp
from jax import lax
from jax.sharding import PartitionSpec as P


def owner_ranks(block_owner, live_slots, dp_count):
    owner_hot = (
        (block_owner[:, None] == jnp.arange(dp_count, dtype=jnp.int32)[None, :])
        & live_slots[:, None]
    ).astype(jnp.int32)
    before = jnp.cumsum(owner_hot, axis=0) - owner_hot
    return jnp.sum(before * owner_hot, axis=1)


def slot_sources(targets, selected, slot_total):
    slot_ids = jnp.arange(slot_total, dtype=jnp.int32)
    chosen = selected[None, :] & (targets[None, :] == slot_ids[:, None])
    entry_ids = jnp.arange(targets.shape[0], dtype=jnp.int32)
    source_index = jnp.sum(jnp.where(chosen, entry_ids[None, :], 0), axis=1).astype(jnp.int32)
    return source_index, jnp.any(chosen, axis=1)


def local_part(table, keep, size_of_chunk):
    def part(c, h):
        rows = lax.dynamic_slice_in_dim(table, c * size_of_chunk, size_of_chunk, 0)[:, h]
        if keep is None:
            return rows
        mask = lax.dynamic_slice_in_dim(keep, c * size_of_chunk, size_of_chunk, 0)
        return jnp.where(mask[:, None, None], rows, 0.0)
    return part


def reduce_owned(grad_sum, block_owner, live_slots, dp_count, owner_cap, row_len, pieces):
    x_count = dp_count // row_len
    half_cap = owner_cap // 2
    rank = owner_ranks(block_owner, live_slots, dp_count)
    owner_x = block_owner // row_len
    owner_z = block_owner % row_len
    half_slots = dp_count * half_cap
    in_a = live_slots & (rank < half_cap)
    in_b = live_slots & (rank >= half_cap)
    target_a = owner_z * (x_count * half_cap) + owner_x * half_cap + rank
    target_b = owner_x * (row_len * half_cap) + owner_z * half_cap + rank - half_cap
    source_a, keep_a = slot_sources(target_a, in_a, half_slots)
    source_b, keep_b = slot_sources(target_b, in_b, half_slots)
    tile = grad_sum.shape[1]
    gathered = jnp.take(grad_sum, jnp.concatenate([source_a, source_b]), axis=0)
    gathered = gathered.reshape((2, half_slots, 2, tile // 2) + grad_sum.shape[2:])
    table_a, table_b = gathered[0], gathered[1]

    dp_me = lax.axis_index("dp")
    me_z = dp_me % row_len
    me_x = dp_me // row_len

    def z_perm(shift):
        return [(i, (i // row_len) * row_len + (i % row_len + shift) % row_len) for i in range(dp_count)]

    def x_perm(shift):
        return [(i, (i + shift * row_len) % dp_count) for i in range(dp_count)]

    z_ring = (row_len, me_z, z_perm)
    x_ring = (x_count, me_x, x_perm)
    plan_a = [(z_ring, local_part(table_a, keep_a, x_count * half_cap)), (x_ring, None)]
    plan_b = [(x_ring, local_part(table_b, keep_b, row_len * half_cap)), (z_ring, None)]

    def start(ring, part):
        size, me, _ = ring
        return [part((me - 1) % size, 0), part((me + 1) % size, 1)]

    def finish(halves):
        return jnp.concatenate([halves[0], halves[1]], axis=1)

    def second_part(row_sum):
        def part(c, h):
            rows = lax.dynamic_slice_in_dim(row_sum, c * half_cap, half_cap, 0)
            return rows[:, h * (tile // 2):(h + 1) * (tile // 2)]
        return part

    rings = [plan_a, plan_b]
    states = []
    for plan in rings:
        (ring1, part1), _ = plan
        states.append({"stage": 0, "k": 0, "halves": start(ring1, part1), "part": part1})
    total_steps = max((p[0][0][0] - 1) + (p[1][0][0] - 1) for p in rings)
    tie_at = {max(1, (total_steps * (i + 1)) // (len(pieces) + 1)): i for i in range(len(pieces))}
    results = [None] * len(pieces)
    for step in range(total_steps):
        received = []
        for plan, st in zip(rings, states):
            ring = plan[st["stage"]][0]
            received.append([
                lax.ppermute(st["halves"][0], "dp", ring[2](1)),
                lax.ppermute(st["halves"][1], "dp", ring[2](-1)),
            ])
        if step in tie_at:
            index = tie_at[step]
            received, results[index] = lax.optimization_barrier((received, pieces[index]()))
        for plan, st, got in zip(rings, states, received):
            size, me, _ = plan[st["stage"]][0]
            k = st["k"]
            part = st["part"]
            st["halves"] = [
                got[0] + part((me - k - 2) % size, 0),
                got[1] + part((me + k + 2) % size, 1),
            ]
            st["k"] = k + 1
            if st["k"] == size - 1 and st["stage"] == 0:
                row_sum = finish(st["halves"])
                ring2 = plan[1][0]
                st["stage"], st["k"] = 1, 0
                st["part"] = second_part(row_sum)
                st["halves"] = start(ring2, st["part"])
    for index in range(len(pieces)):
        if results[index] is None:
            results[index] = pieces[index]()
    owned = jnp.concatenate([finish(states[0]["halves"]), finish(states[1]["halves"])], axis=0)
    return owned, results


def gather_columns(upstream, mp_count):
    me = lax.axis_index("mp")
    width = upstream.shape[2] // mp_count
    pieces = [None] * mp_count
    for shift in range(mp_count):
        target = (me + shift) % mp_count
        piece = lax.dynamic_slice_in_dim(upstream, target * width, width, 2)
        if shift:
            perm = [(m, (m + shift) % mp_count) for m in range(mp_count)]
            piece = lax.ppermute(piece, "mp", perm)
        pieces[shift] = piece
    stacked = jnp.stack(pieces, axis=0)
    shift_of_source = (me - jnp.arange(mp_count, dtype=jnp.int32)) % mp_count
    ordered = jnp.take(stacked, shift_of_source, axis=0)
    return ordered.reshape((mp_count * upstream.shape[0],) + upstream.shape[1:2] + (width,))


def local(tokens, upstream, deltas, block_row, block_column, block_owner, block_count):
    model_width = tokens.shape[1]
    tile_size = deltas.shape[1]
    slot_count = deltas.shape[0]
    mp_count = lax.axis_size("mp")
    dp_count = lax.axis_size("dp")
    hidden = gather_columns(upstream, mp_count)
    group_rows = hidden.shape[0]
    column_blocks = hidden.shape[1] * hidden.shape[2] // tile_size
    hidden_major = jnp.transpose(hidden.reshape(group_rows, column_blocks, tile_size), (1, 0, 2))
    upstream_chosen = jnp.take(hidden_major, block_column, axis=0)
    slot_ids = jnp.arange(slot_count, dtype=jnp.int32)
    live_slots = slot_ids < block_count[0]
    column_table = (
        live_slots[:, None]
        & (block_column[:, None] == jnp.arange(column_blocks, dtype=jnp.int32)[None, :])
    ).astype(jnp.float32)
    shard_rows = lax.all_gather(tokens, "mp", axis=0, tiled=True)
    row_count = shard_rows.shape[0]
    row_major = jnp.transpose(
        shard_rows.reshape(row_count, model_width // tile_size, tile_size), (1, 0, 2)
    )
    feature_tiles = jnp.take(row_major, block_row, axis=0)
    grad_sum = jnp.einsum(
        "kni,kno->kio", feature_tiles, upstream_chosen, preferred_element_type=jnp.float32
    )
    owner_cap = 3 * slot_count // (2 * dp_count)
    row_len = 8 if dp_count % 8 == 0 else dp_count
    piece_count = 4
    piece_rows = group_rows // piece_count

    def branch_piece(i):
        def run():
            rows_in = feature_tiles[:, i * piece_rows:(i + 1) * piece_rows]
            product = jnp.einsum("kni,kio->kno", rows_in, deltas, preferred_element_type=jnp.float32)
            rows_out = jnp.einsum("kc,kno->cno", column_table, product, precision=lax.Precision.HIGHEST)
            return jnp.transpose(rows_out.astype(jnp.bfloat16), (1, 0, 2)).reshape(
                piece_rows, hidden.shape[1], hidden.shape[2]
            )
        return run

    owned, branch_parts = reduce_owned(
        grad_sum, block_owner, live_slots, dp_count, owner_cap, row_len,
        [branch_piece(i) for i in range(piece_count)],
    )
    branch_out = jnp.concatenate(branch_parts, axis=0)
    return (branch_out, owned[None])


def solution(mesh):
    placed = (
        P(("dp", "mp"), None),
        P(("dp", "mp"), None, None),
        P("mp", None, None),
        P("mp"),
        P("mp"),
        P("mp"),
        P("mp"),
    )
    return jax.shard_map(
        local,
        mesh=mesh,
        in_specs=placed,
        out_specs=(P("dp", None, "mp"), P("mp", "dp", None, None)),
        check_vma=False,
    )
```

```python
import jax
import jax.numpy as jnp
from jax import lax
from jax.sharding import PartitionSpec as P


def owner_ranks(block_owner, live_slots, dp_count):
    owner_hot = (
        (block_owner[:, None] == jnp.arange(dp_count, dtype=jnp.int32)[None, :])
        & live_slots[:, None]
    ).astype(jnp.int32)
    before = jnp.cumsum(owner_hot, axis=0) - owner_hot
    return jnp.sum(before * owner_hot, axis=1)


def slot_sources(targets, selected, slot_total):
    slot_ids = jnp.arange(slot_total, dtype=jnp.int32)
    chosen = selected[None, :] & (targets[None, :] == slot_ids[:, None])
    entry_ids = jnp.arange(targets.shape[0], dtype=jnp.int32)
    source_index = jnp.sum(jnp.where(chosen, entry_ids[None, :], 0), axis=1).astype(jnp.int32)
    return source_index, jnp.any(chosen, axis=1)


def local_part(table, keep, size_of_chunk):
    def part(c, h):
        rows = lax.dynamic_slice_in_dim(table, c * size_of_chunk, size_of_chunk, 0)
        half = rows.shape[1] // 2
        rows = rows[:, h * half:(h + 1) * half]
        if keep is None:
            return rows
        mask = lax.dynamic_slice_in_dim(keep, c * size_of_chunk, size_of_chunk, 0)
        return jnp.where(mask[:, None, None], rows, 0.0)
    return part


def reduce_owned(grad_sum, block_owner, live_slots, dp_count, owner_cap, row_len, pieces):
    x_count = dp_count // row_len
    half_cap = owner_cap // 2
    rank = owner_ranks(block_owner, live_slots, dp_count)
    owner_x = block_owner // row_len
    owner_z = block_owner % row_len
    half_slots = dp_count * half_cap
    in_a = live_slots & (rank < half_cap)
    in_b = live_slots & (rank >= half_cap)
    target_a = owner_z * (x_count * half_cap) + owner_x * half_cap + rank
    target_b = owner_x * (row_len * half_cap) + owner_z * half_cap + rank - half_cap
    source_a, keep_a = slot_sources(target_a, in_a, half_slots)
    source_b, keep_b = slot_sources(target_b, in_b, half_slots)
    tile = grad_sum.shape[1]
    table_a = jnp.take(grad_sum, source_a, axis=0, mode="clip")
    table_b = jnp.take(grad_sum, source_b, axis=0, mode="clip")

    dp_me = lax.axis_index("dp")
    me_z = dp_me % row_len
    me_x = dp_me // row_len

    def z_perm(shift):
        return [(i, (i // row_len) * row_len + (i % row_len + shift) % row_len) for i in range(dp_count)]

    def x_perm(shift):
        return [(i, (i + shift * row_len) % dp_count) for i in range(dp_count)]

    z_ring = (row_len, me_z, z_perm)
    x_ring = (x_count, me_x, x_perm)
    plan_a = [(z_ring, local_part(table_a, keep_a, x_count * half_cap)), (x_ring, None)]
    plan_b = [(x_ring, local_part(table_b, keep_b, row_len * half_cap)), (z_ring, None)]

    def start(ring, part):
        size, me, _ = ring
        return [part((me - 1) % size, 0), part((me + 1) % size, 1)]

    def finish(halves):
        return jnp.concatenate([halves[0], halves[1]], axis=1)

    def second_part(row_sum):
        def part(c, h):
            rows = lax.dynamic_slice_in_dim(row_sum, c * half_cap, half_cap, 0)
            return rows[:, h * (tile // 2):(h + 1) * (tile // 2)]
        return part

    rings = [plan_a, plan_b]
    states = []
    for plan in rings:
        (ring1, part1), _ = plan
        states.append({"stage": 0, "k": 0, "halves": start(ring1, part1), "part": part1})
    total_steps = max((p[0][0][0] - 1) + (p[1][0][0] - 1) for p in rings)
    tie_at = {max(1, (total_steps * (i + 1)) // (len(pieces) + 1)): i for i in range(len(pieces))}
    results = [None] * len(pieces)
    for step in range(total_steps):
        received = []
        for plan, st in zip(rings, states):
            ring = plan[st["stage"]][0]
            received.append([
                lax.ppermute(st["halves"][0], "dp", ring[2](1)),
                lax.ppermute(st["halves"][1], "dp", ring[2](-1)),
            ])
        if step in tie_at:
            index = tie_at[step]
            received, results[index] = lax.optimization_barrier((received, pieces[index]()))
        for plan, st, got in zip(rings, states, received):
            size, me, _ = plan[st["stage"]][0]
            k = st["k"]
            part = st["part"]
            st["halves"] = [
                got[0] + part((me - k - 2) % size, 0),
                got[1] + part((me + k + 2) % size, 1),
            ]
            st["k"] = k + 1
            if st["k"] == size - 1 and st["stage"] == 0:
                row_sum = finish(st["halves"])
                ring2 = plan[1][0]
                st["stage"], st["k"] = 1, 0
                st["part"] = second_part(row_sum)
                st["halves"] = start(ring2, st["part"])
    for index in range(len(pieces)):
        if results[index] is None:
            results[index] = pieces[index]()
    owned = jnp.concatenate([finish(states[0]["halves"]), finish(states[1]["halves"])], axis=0)
    return owned, results


def gather_columns(upstream, mp_count):
    me = lax.axis_index("mp")
    width = upstream.shape[2] // mp_count
    pieces = [None] * mp_count
    for shift in range(mp_count):
        target = (me + shift) % mp_count
        piece = lax.dynamic_slice_in_dim(upstream, target * width, width, 2)
        if shift:
            perm = [(m, (m + shift) % mp_count) for m in range(mp_count)]
            piece = lax.ppermute(piece, "mp", perm)
        pieces[shift] = piece
    ordered = jnp.zeros((mp_count,) + pieces[0].shape, pieces[0].dtype)
    for shift in range(mp_count):
        ordered = lax.dynamic_update_index_in_dim(ordered, pieces[shift], (me - shift) % mp_count, 0)
    return ordered.reshape((mp_count * upstream.shape[0],) + upstream.shape[1:2] + (width,))


def local(tokens, upstream, deltas, block_row, block_column, block_owner, block_count):
    model_width = tokens.shape[1]
    tile_size = deltas.shape[1]
    slot_count = deltas.shape[0]
    mp_count = lax.axis_size("mp")
    dp_count = lax.axis_size("dp")
    hidden = gather_columns(upstream, mp_count)
    group_rows = hidden.shape[0]
    column_blocks = hidden.shape[1] * hidden.shape[2] // tile_size
    hidden_major = jnp.transpose(hidden.reshape(group_rows, column_blocks, tile_size), (1, 0, 2))
    upstream_chosen = jnp.take(hidden_major, block_column, axis=0, mode="clip")
    slot_ids = jnp.arange(slot_count, dtype=jnp.int32)
    live_slots = slot_ids < block_count[0]
    column_table = (
        live_slots[:, None]
        & (block_column[:, None] == jnp.arange(column_blocks, dtype=jnp.int32)[None, :])
    ).astype(jnp.float32)
    shard_rows = lax.all_gather(tokens, "mp", axis=0, tiled=True)
    row_count = shard_rows.shape[0]
    row_major = jnp.transpose(
        shard_rows.reshape(row_count, model_width // tile_size, tile_size), (1, 0, 2)
    )
    feature_tiles = jnp.take(row_major, block_row, axis=0, mode="clip")
    grad_sum = jnp.einsum(
        "kni,kno->kio", feature_tiles, upstream_chosen, preferred_element_type=jnp.float32
    )
    owner_cap = 3 * slot_count // (2 * dp_count)
    row_len = 8 if dp_count % 8 == 0 else dp_count
    piece_count = 4
    piece_rows = group_rows // piece_count

    def branch_piece(i):
        def run():
            rows_in = feature_tiles[:, i * piece_rows:(i + 1) * piece_rows]
            product = jnp.einsum("kni,kio->kno", rows_in, deltas, preferred_element_type=jnp.float32)
            rows_out = jnp.einsum("kc,kno->cno", column_table, product, precision=lax.Precision.HIGHEST)
            return jnp.transpose(rows_out.astype(jnp.bfloat16), (1, 0, 2)).reshape(
                piece_rows, hidden.shape[1], hidden.shape[2]
            )
        return run

    owned, branch_parts = reduce_owned(
        grad_sum, block_owner, live_slots, dp_count, owner_cap, row_len,
        [branch_piece(i) for i in range(piece_count)],
    )
    branch_out = jnp.concatenate(branch_parts, axis=0)
    return (branch_out, owned[None])


def solution(mesh):
    placed = (
        P(("dp", "mp"), None),
        P(("dp", "mp"), None, None),
        P("mp", None, None),
        P("mp"),
        P("mp"),
        P("mp"),
        P("mp"),
    )
    return jax.shard_map(
        local,
        mesh=mesh,
        in_specs=placed,
        out_specs=(P("dp", None, "mp"), P("mp", "dp", None, None)),
        check_vma=False,
    )
```

```python
import jax
import jax.numpy as jnp
from jax import lax
from jax.sharding import PartitionSpec as P


def owner_ranks(block_owner, live_slots, dp_count):
    owner_hot = (
        (block_owner[:, None] == jnp.arange(dp_count, dtype=jnp.int32)[None, :])
        & live_slots[:, None]
    ).astype(jnp.int32)
    before = jnp.cumsum(owner_hot, axis=0) - owner_hot
    return jnp.sum(before * owner_hot, axis=1)


def slot_sources(targets, selected, slot_total):
    slot_ids = jnp.arange(slot_total, dtype=jnp.int32)
    chosen = selected[None, :] & (targets[None, :] == slot_ids[:, None])
    entry_ids = jnp.arange(targets.shape[0], dtype=jnp.int32)
    source_index = jnp.sum(jnp.where(chosen, entry_ids[None, :], 0), axis=1).astype(jnp.int32)
    return source_index, jnp.any(chosen, axis=1)


def local_part(table, keep, size_of_chunk):
    def part(c, h):
        rows = lax.dynamic_slice_in_dim(table, c * size_of_chunk, size_of_chunk, 0)
        half = rows.shape[1] // 2
        rows = rows[:, h * half:(h + 1) * half]
        if keep is None:
            return rows
        mask = lax.dynamic_slice_in_dim(keep, c * size_of_chunk, size_of_chunk, 0)
        return jnp.where(mask[:, None, None], rows, 0.0)
    return part


def reduce_owned(grad_sum, block_owner, live_slots, dp_count, owner_cap, row_len, pieces, join):
    x_count = dp_count // row_len
    half_cap = owner_cap // 2
    rank = owner_ranks(block_owner, live_slots, dp_count)
    owner_x = block_owner // row_len
    owner_z = block_owner % row_len
    half_slots = dp_count * half_cap
    in_a = live_slots & (rank < half_cap)
    in_b = live_slots & (rank >= half_cap)
    target_a = owner_z * (x_count * half_cap) + owner_x * half_cap + rank
    target_b = owner_x * (row_len * half_cap) + owner_z * half_cap + rank - half_cap
    source_a, keep_a = slot_sources(target_a, in_a, half_slots)
    source_b, keep_b = slot_sources(target_b, in_b, half_slots)
    tile = grad_sum.shape[1]
    table_a = jnp.take(grad_sum, source_a, axis=0, mode="clip")
    table_b = jnp.take(grad_sum, source_b, axis=0, mode="clip")

    dp_me = lax.axis_index("dp")
    me_z = dp_me % row_len
    me_x = dp_me // row_len

    def z_perm(shift):
        return [(i, (i // row_len) * row_len + (i % row_len + shift) % row_len) for i in range(dp_count)]

    def x_perm(shift):
        return [(i, (i + shift * row_len) % dp_count) for i in range(dp_count)]

    z_ring = (row_len, me_z, z_perm)
    x_ring = (x_count, me_x, x_perm)
    plan_a = [(z_ring, local_part(table_a, keep_a, x_count * half_cap)), (x_ring, None)]
    plan_b = [(x_ring, local_part(table_b, keep_b, row_len * half_cap)), (z_ring, None)]

    def start(ring, part):
        size, me, _ = ring
        return [part((me - 1) % size, 0), part((me + 1) % size, 1)]

    def finish(halves):
        return jnp.concatenate([halves[0], halves[1]], axis=1)

    def second_part(row_sum):
        def part(c, h):
            rows = lax.dynamic_slice_in_dim(row_sum, c * half_cap, half_cap, 0)
            return rows[:, h * (tile // 2):(h + 1) * (tile // 2)]
        return part

    rings = [plan_a, plan_b]
    states = []
    for plan in rings:
        (ring1, part1), _ = plan
        states.append({"stage": 0, "k": 0, "halves": start(ring1, part1), "part": part1})
    total_steps = max((p[0][0][0] - 1) + (p[1][0][0] - 1) for p in rings)
    tie_at = {i: i for i in range(len(pieces))}
    results = [None] * len(pieces)
    for step in range(total_steps):
        received = []
        for plan, st in zip(rings, states):
            ring = plan[st["stage"]][0]
            received.append([
                lax.ppermute(st["halves"][0], "dp", ring[2](1)),
                lax.ppermute(st["halves"][1], "dp", ring[2](-1)),
            ])
        if step in tie_at:
            index = tie_at[step]
            received, results[index] = lax.optimization_barrier((received, pieces[index]()))
        if step == len(pieces):
            received, joined = lax.optimization_barrier((received, join(results)))
        for plan, st, got in zip(rings, states, received):
            size, me, _ = plan[st["stage"]][0]
            k = st["k"]
            part = st["part"]
            st["halves"] = [
                got[0] + part((me - k - 2) % size, 0),
                got[1] + part((me + k + 2) % size, 1),
            ]
            st["k"] = k + 1
            if st["k"] == size - 1 and st["stage"] == 0:
                row_sum = finish(st["halves"])
                ring2 = plan[1][0]
                st["stage"], st["k"] = 1, 0
                st["part"] = second_part(row_sum)
                st["halves"] = start(ring2, st["part"])
    if total_steps <= len(pieces):
        joined = join([part() if done is None else done for part, done in zip(pieces, results)])
    owned = jnp.concatenate([finish(states[0]["halves"]), finish(states[1]["halves"])], axis=0)
    return owned, joined


def gather_columns(upstream, mp_count, carry):
    me = lax.axis_index("mp")
    width = upstream.shape[2] // mp_count
    pieces = [None] * mp_count
    for shift in range(mp_count):
        target = (me + shift) % mp_count
        piece = lax.dynamic_slice_in_dim(upstream, target * width, width, 2)
        if shift:
            perm = [(m, (m + shift) % mp_count) for m in range(mp_count)]
            piece = lax.ppermute(piece, "mp", perm)
        pieces[shift] = piece
    pieces, carry = lax.optimization_barrier((pieces, carry))
    ordered = jnp.zeros((mp_count,) + pieces[0].shape, pieces[0].dtype)
    for shift in range(mp_count):
        ordered = lax.dynamic_update_index_in_dim(ordered, pieces[shift], (me - shift) % mp_count, 0)
    return ordered.reshape((mp_count * upstream.shape[0],) + upstream.shape[1:2] + (width,)), carry


def local(tokens, upstream, deltas, block_row, block_column, block_owner, block_count):
    model_width = tokens.shape[1]
    tile_size = deltas.shape[1]
    slot_count = deltas.shape[0]
    mp_count = lax.axis_size("mp")
    dp_count = lax.axis_size("dp")
    shard_rows = lax.all_gather(tokens, "mp", axis=0, tiled=True)
    row_count = shard_rows.shape[0]
    row_major = jnp.transpose(
        shard_rows.reshape(row_count, model_width // tile_size, tile_size), (1, 0, 2)
    )
    feature_tiles = jnp.take(row_major, block_row, axis=0, mode="clip")
    hidden, feature_tiles = gather_columns(upstream, mp_count, feature_tiles)
    group_rows = hidden.shape[0]
    column_blocks = hidden.shape[1] * hidden.shape[2] // tile_size
    hidden_major = jnp.transpose(hidden.reshape(group_rows, column_blocks, tile_size), (1, 0, 2))
    upstream_chosen = jnp.take(hidden_major, block_column, axis=0, mode="clip")
    slot_ids = jnp.arange(slot_count, dtype=jnp.int32)
    live_slots = slot_ids < block_count[0]
    column_table = (
        live_slots[:, None]
        & (block_column[:, None] == jnp.arange(column_blocks, dtype=jnp.int32)[None, :])
    ).astype(jnp.float32)
    grad_sum = jnp.einsum(
        "kni,kno->kio", feature_tiles, upstream_chosen, preferred_element_type=jnp.float32
    )
    owner_cap = 3 * slot_count // (2 * dp_count)
    row_len = 8 if dp_count % 8 == 0 else dp_count
    piece_count = 4
    piece_rows = group_rows // piece_count

    def branch_piece(i):
        def run():
            rows_in = feature_tiles[:, i * piece_rows:(i + 1) * piece_rows]
            product = jnp.einsum("kni,kio->kno", rows_in, deltas, preferred_element_type=jnp.float32)
            rows_out = jnp.einsum("kc,kno->cno", column_table, product, precision=lax.Precision.HIGHEST)
            return jnp.transpose(rows_out.astype(jnp.bfloat16), (1, 0, 2)).reshape(
                piece_rows, hidden.shape[1], hidden.shape[2]
            )
        return run

    owned, branch_out = reduce_owned(
        grad_sum, block_owner, live_slots, dp_count, owner_cap, row_len,
        [branch_piece(i) for i in range(piece_count)],
        lambda parts: jnp.concatenate(parts, axis=0),
    )
    return (branch_out, owned[None])


def solution(mesh):
    placed = (
        P(("dp", "mp"), None),
        P(("dp", "mp"), None, None),
        P("mp", None, None),
        P("mp"),
        P("mp"),
        P("mp"),
        P("mp"),
    )
    return jax.shard_map(
        local,
        mesh=mesh,
        in_specs=placed,
        out_specs=(P("dp", None, "mp"), P("mp", "dp", None, None)),
        check_vma=False,
    )
```

```python
import jax
import jax.numpy as jnp
from jax import lax
from jax.sharding import PartitionSpec as P


def owner_ranks(block_owner, live_slots, dp_count):
    owner_hot = (
        (block_owner[:, None] == jnp.arange(dp_count, dtype=jnp.int32)[None, :])
        & live_slots[:, None]
    ).astype(jnp.int32)
    before = jnp.cumsum(owner_hot, axis=0) - owner_hot
    return jnp.sum(before * owner_hot, axis=1)


def slot_sources(targets, selected, slot_total):
    slot_ids = jnp.arange(slot_total, dtype=jnp.int32)
    chosen = selected[None, :] & (targets[None, :] == slot_ids[:, None])
    entry_ids = jnp.arange(targets.shape[0], dtype=jnp.int32)
    source_index = jnp.sum(jnp.where(chosen, entry_ids[None, :], 0), axis=1).astype(jnp.int32)
    return source_index, jnp.any(chosen, axis=1)


def local_part(table, keep, size_of_chunk):
    def part(c, h):
        rows = lax.dynamic_slice_in_dim(table, c * size_of_chunk, size_of_chunk, 0)
        half = rows.shape[1] // 2
        rows = rows[:, h * half:(h + 1) * half]
        if keep is None:
            return rows
        mask = lax.dynamic_slice_in_dim(keep, c * size_of_chunk, size_of_chunk, 0)
        return jnp.where(mask[:, None, None], rows, 0.0)
    return part


def reduce_owned(grad_sum, block_owner, live_slots, dp_count, owner_cap, row_len, pieces, join):
    x_count = dp_count // row_len
    half_cap = owner_cap // 2
    rank = owner_ranks(block_owner, live_slots, dp_count)
    owner_x = block_owner // row_len
    owner_z = block_owner % row_len
    half_slots = dp_count * half_cap
    in_a = live_slots & (rank < half_cap)
    in_b = live_slots & (rank >= half_cap)
    target_a = owner_z * (x_count * half_cap) + owner_x * half_cap + rank
    target_b = owner_x * (row_len * half_cap) + owner_z * half_cap + rank - half_cap
    source_a, keep_a = slot_sources(target_a, in_a, half_slots)
    source_b, keep_b = slot_sources(target_b, in_b, half_slots)
    tile = grad_sum.shape[1]
    table_a = jnp.take(grad_sum, source_a, axis=0, mode="clip")
    table_b = jnp.take(grad_sum, source_b, axis=0, mode="clip")

    dp_me = lax.axis_index("dp")
    me_z = dp_me % row_len
    me_x = dp_me // row_len

    def z_perm(shift):
        return [(i, (i // row_len) * row_len + (i % row_len + shift) % row_len) for i in range(dp_count)]

    def x_perm(shift):
        return [(i, (i + shift * row_len) % dp_count) for i in range(dp_count)]

    z_ring = (row_len, me_z, z_perm)
    x_ring = (x_count, me_x, x_perm)
    plan_a = [(z_ring, local_part(table_a, keep_a, x_count * half_cap)), (x_ring, None)]
    plan_b = [(x_ring, local_part(table_b, keep_b, row_len * half_cap)), (z_ring, None)]

    def start(ring, part):
        size, me, _ = ring
        return [part((me - 1) % size, 0), part((me + 1) % size, 1)]

    def finish(halves):
        return jnp.concatenate([halves[0], halves[1]], axis=1)

    def second_part(row_sum):
        def part(c, h):
            rows = lax.dynamic_slice_in_dim(row_sum, c * half_cap, half_cap, 0)
            return rows[:, h * (tile // 2):(h + 1) * (tile // 2)]
        return part

    rings = [plan_a, plan_b]
    states = []
    for plan in rings:
        (ring1, part1), _ = plan
        states.append({"stage": 0, "k": 0, "halves": start(ring1, part1), "part": part1})
    total_steps = max((p[0][0][0] - 1) + (p[1][0][0] - 1) for p in rings)
    tie_at = {i: i for i in range(len(pieces))}
    results = [None] * len(pieces)
    for step in range(total_steps):
        received = []
        for plan, st in zip(rings, states):
            ring = plan[st["stage"]][0]
            received.append([
                lax.ppermute(st["halves"][0], "dp", ring[2](1)),
                lax.ppermute(st["halves"][1], "dp", ring[2](-1)),
            ])
        if step in tie_at:
            index = tie_at[step]
            received, results[index] = lax.optimization_barrier((received, pieces[index]()))
        if step == len(pieces):
            received, joined = lax.optimization_barrier((received, join(results)))
        for plan, st, got in zip(rings, states, received):
            size, me, _ = plan[st["stage"]][0]
            k = st["k"]
            part = st["part"]
            st["halves"] = [
                got[0] + part((me - k - 2) % size, 0),
                got[1] + part((me + k + 2) % size, 1),
            ]
            st["k"] = k + 1
            if st["k"] == size - 1 and st["stage"] == 0:
                row_sum = finish(st["halves"])
                ring2 = plan[1][0]
                st["stage"], st["k"] = 1, 0
                st["part"] = second_part(row_sum)
                st["halves"] = start(ring2, st["part"])
    if total_steps <= len(pieces):
        joined = join([part() if done is None else done for part, done in zip(pieces, results)])
    owned = jnp.concatenate([finish(states[0]["halves"]), finish(states[1]["halves"])], axis=0)
    return owned, joined


def gather_columns(upstream, mp_count):
    me = lax.axis_index("mp")
    width = upstream.shape[2] // mp_count
    pieces = [None] * mp_count
    for shift in range(mp_count):
        target = (me + shift) % mp_count
        piece = lax.dynamic_slice_in_dim(upstream, target * width, width, 2)
        if shift:
            perm = [(m, (m + shift) % mp_count) for m in range(mp_count)]
            piece = lax.ppermute(piece, "mp", perm)
        pieces[shift] = piece
    ordered = jnp.zeros((mp_count,) + pieces[0].shape, pieces[0].dtype)
    for shift in range(mp_count):
        ordered = lax.dynamic_update_index_in_dim(ordered, pieces[shift], (me - shift) % mp_count, 0)
    return ordered.reshape((mp_count * upstream.shape[0],) + upstream.shape[1:2] + (width,))


def local(tokens, upstream, deltas, block_row, block_column, block_owner, block_count):
    model_width = tokens.shape[1]
    tile_size = deltas.shape[1]
    slot_count = deltas.shape[0]
    mp_count = lax.axis_size("mp")
    dp_count = lax.axis_size("dp")
    hidden = gather_columns(upstream, mp_count)
    group_rows = hidden.shape[0]
    column_blocks = hidden.shape[1] * hidden.shape[2] // tile_size
    hidden_major = jnp.transpose(hidden.reshape(group_rows, column_blocks, tile_size), (1, 0, 2))
    upstream_chosen = jnp.take(hidden_major, block_column, axis=0, mode="clip")
    slot_ids = jnp.arange(slot_count, dtype=jnp.int32)
    live_slots = slot_ids < block_count[0]
    column_table = (
        live_slots[:, None]
        & (block_column[:, None] == jnp.arange(column_blocks, dtype=jnp.int32)[None, :])
    ).astype(jnp.float32)
    shard_rows = lax.all_gather(tokens, "mp", axis=0, tiled=True)
    row_count = shard_rows.shape[0]
    row_major = jnp.transpose(
        shard_rows.reshape(row_count, model_width // tile_size, tile_size), (1, 0, 2)
    )
    feature_tiles = jnp.take(row_major, block_row, axis=0, mode="clip")
    grad_sum = jnp.einsum(
        "kni,kno->kio", feature_tiles, upstream_chosen, preferred_element_type=jnp.float32
    )
    owner_cap = 3 * slot_count // (2 * dp_count)
    row_len = 8 if dp_count % 8 == 0 else dp_count
    piece_count = 4
    piece_rows = group_rows // piece_count

    def branch_piece(i):
        def run():
            rows_in = feature_tiles[:, i * piece_rows:(i + 1) * piece_rows]
            product = jnp.einsum("kni,kio->kno", rows_in, deltas, preferred_element_type=jnp.float32)
            rows_out = jnp.einsum("kc,kno->cno", column_table, product, precision=lax.Precision.HIGHEST)
            return jnp.transpose(rows_out.astype(jnp.bfloat16), (1, 0, 2)).reshape(
                piece_rows, hidden.shape[1], hidden.shape[2]
            )
        return run

    owned, branch_out = reduce_owned(
        grad_sum, block_owner, live_slots, dp_count, owner_cap, row_len,
        [branch_piece(i) for i in range(piece_count)],
        lambda parts: jnp.concatenate(parts, axis=0),
    )
    return (branch_out, owned[None])


def solution(mesh):
    placed = (
        P(("dp", "mp"), None),
        P(("dp", "mp"), None, None),
        P("mp", None, None),
        P("mp"),
        P("mp"),
        P("mp"),
        P("mp"),
    )
    return jax.shard_map(
        local,
        mesh=mesh,
        in_specs=placed,
        out_specs=(P("dp", None, "mp"), P("mp", "dp", None, None)),
        check_vma=False,
    )
```

```python
import jax
import jax.numpy as jnp
from jax import lax
from jax.sharding import PartitionSpec as P


def owner_ranks(block_owner, live_slots, dp_count):
    owner_hot = (
        (block_owner[:, None] == jnp.arange(dp_count, dtype=jnp.int32)[None, :])
        & live_slots[:, None]
    ).astype(jnp.int32)
    before = jnp.cumsum(owner_hot, axis=0) - owner_hot
    return jnp.sum(before * owner_hot, axis=1)


def slot_sources(targets, selected, slot_total):
    slot_ids = jnp.arange(slot_total, dtype=jnp.int32)
    chosen = selected[None, :] & (targets[None, :] == slot_ids[:, None])
    entry_ids = jnp.arange(targets.shape[0], dtype=jnp.int32)
    source_index = jnp.sum(jnp.where(chosen, entry_ids[None, :], 0), axis=1).astype(jnp.int32)
    return source_index, jnp.any(chosen, axis=1)


def local_part(table, keep, size_of_chunk):
    def part(c, h):
        rows = lax.dynamic_slice_in_dim(table, c * size_of_chunk, size_of_chunk, 0)
        half = rows.shape[1] // 2
        rows = rows[:, h * half:(h + 1) * half]
        if keep is None:
            return rows
        mask = lax.dynamic_slice_in_dim(keep, c * size_of_chunk, size_of_chunk, 0)
        return jnp.where(mask[:, None, None], rows, 0.0)
    return part


def reduce_owned(grad_sum, block_owner, live_slots, dp_count, owner_cap, row_len, pieces, join):
    x_count = dp_count // row_len
    half_cap = owner_cap // 2
    rank = owner_ranks(block_owner, live_slots, dp_count)
    owner_x = block_owner // row_len
    owner_z = block_owner % row_len
    half_slots = dp_count * half_cap
    in_a = live_slots & (rank < half_cap)
    in_b = live_slots & (rank >= half_cap)
    target_a = owner_z * (x_count * half_cap) + owner_x * half_cap + rank
    target_b = owner_x * (row_len * half_cap) + owner_z * half_cap + rank - half_cap
    source_a, keep_a = slot_sources(target_a, in_a, half_slots)
    source_b, keep_b = slot_sources(target_b, in_b, half_slots)
    tile = grad_sum.shape[1]
    table_a = jnp.take(grad_sum, source_a, axis=0, mode="clip")
    table_b = jnp.take(grad_sum, source_b, axis=0, mode="clip")

    dp_me = lax.axis_index("dp")
    me_z = dp_me % row_len
    me_x = dp_me // row_len

    def z_perm(shift):
        return [(i, (i // row_len) * row_len + (i % row_len + shift) % row_len) for i in range(dp_count)]

    def x_perm(shift):
        return [(i, (i + shift * row_len) % dp_count) for i in range(dp_count)]

    z_ring = (row_len, me_z, z_perm)
    x_ring = (x_count, me_x, x_perm)
    plan_a = [(z_ring, local_part(table_a, keep_a, x_count * half_cap)), (x_ring, None)]
    plan_b = [(x_ring, local_part(table_b, keep_b, row_len * half_cap)), (z_ring, None)]

    def start(ring, part):
        size, me, _ = ring
        return [part((me - 1) % size, 0), part((me + 1) % size, 1)]

    def finish(halves):
        return jnp.concatenate([halves[0], halves[1]], axis=1)

    def second_part(row_sum):
        def part(c, h):
            rows = lax.dynamic_slice_in_dim(row_sum, c * half_cap, half_cap, 0)
            return rows[:, h * (tile // 2):(h + 1) * (tile // 2)]
        return part

    rings = [plan_a, plan_b]
    states = []
    for plan in rings:
        (ring1, part1), _ = plan
        states.append({"stage": 0, "k": 0, "halves": start(ring1, part1), "part": part1})
    total_steps = max((p[0][0][0] - 1) + (p[1][0][0] - 1) for p in rings)
    first_tie = 2
    tie_at = {i + first_tie: i for i in range(len(pieces))}
    results = [None] * len(pieces)
    for step in range(total_steps):
        received = []
        for plan, st in zip(rings, states):
            ring = plan[st["stage"]][0]
            received.append([
                lax.ppermute(st["halves"][0], "dp", ring[2](1)),
                lax.ppermute(st["halves"][1], "dp", ring[2](-1)),
            ])
        if step in tie_at:
            index = tie_at[step]
            received, results[index] = lax.optimization_barrier((received, pieces[index]()))
        if step == len(pieces) + first_tie:
            received, joined = lax.optimization_barrier((received, join(results)))
        for plan, st, got in zip(rings, states, received):
            size, me, _ = plan[st["stage"]][0]
            k = st["k"]
            part = st["part"]
            st["halves"] = [
                got[0] + part((me - k - 2) % size, 0),
                got[1] + part((me + k + 2) % size, 1),
            ]
            st["k"] = k + 1
            if st["k"] == size - 1 and st["stage"] == 0:
                row_sum = finish(st["halves"])
                ring2 = plan[1][0]
                st["stage"], st["k"] = 1, 0
                st["part"] = second_part(row_sum)
                st["halves"] = start(ring2, st["part"])
    if total_steps <= len(pieces) + first_tie:
        joined = join([part() if done is None else done for part, done in zip(pieces, results)])
    owned = jnp.concatenate([finish(states[0]["halves"]), finish(states[1]["halves"])], axis=0)
    return owned, joined


def gather_columns(upstream, mp_count):
    me = lax.axis_index("mp")
    width = upstream.shape[2] // mp_count
    pieces = [None] * mp_count
    for shift in range(mp_count):
        target = (me + shift) % mp_count
        piece = lax.dynamic_slice_in_dim(upstream, target * width, width, 2)
        if shift:
            perm = [(m, (m + shift) % mp_count) for m in range(mp_count)]
            piece = lax.ppermute(piece, "mp", perm)
        pieces[shift] = piece
    ordered = jnp.zeros((mp_count,) + pieces[0].shape, pieces[0].dtype)
    for shift in range(mp_count):
        ordered = lax.dynamic_update_index_in_dim(ordered, pieces[shift], (me - shift) % mp_count, 0)
    return ordered.reshape((mp_count * upstream.shape[0],) + upstream.shape[1:2] + (width,))


def local(tokens, upstream, deltas, block_row, block_column, block_owner, block_count):
    model_width = tokens.shape[1]
    tile_size = deltas.shape[1]
    slot_count = deltas.shape[0]
    mp_count = lax.axis_size("mp")
    dp_count = lax.axis_size("dp")
    hidden = gather_columns(upstream, mp_count)
    group_rows = hidden.shape[0]
    column_blocks = hidden.shape[1] * hidden.shape[2] // tile_size
    hidden_major = jnp.transpose(hidden.reshape(group_rows, column_blocks, tile_size), (1, 0, 2))
    upstream_chosen = jnp.take(hidden_major, block_column, axis=0, mode="clip")
    slot_ids = jnp.arange(slot_count, dtype=jnp.int32)
    live_slots = slot_ids < block_count[0]
    column_table = (
        live_slots[:, None]
        & (block_column[:, None] == jnp.arange(column_blocks, dtype=jnp.int32)[None, :])
    ).astype(jnp.float32)
    shard_rows = lax.all_gather(tokens, "mp", axis=0, tiled=True)
    row_count = shard_rows.shape[0]
    row_major = jnp.transpose(
        shard_rows.reshape(row_count, model_width // tile_size, tile_size), (1, 0, 2)
    )
    feature_tiles = jnp.take(row_major, block_row, axis=0, mode="clip")
    grad_sum = jnp.einsum(
        "kni,kno->kio", feature_tiles, upstream_chosen, preferred_element_type=jnp.float32
    )
    owner_cap = 3 * slot_count // (2 * dp_count)
    row_len = 8 if dp_count % 8 == 0 else dp_count
    piece_count = 4
    piece_rows = group_rows // piece_count

    def branch_piece(i):
        def run():
            rows_in = feature_tiles[:, i * piece_rows:(i + 1) * piece_rows]
            product = jnp.einsum("kni,kio->kno", rows_in, deltas, preferred_element_type=jnp.float32)
            rows_out = jnp.einsum("kc,kno->cno", column_table, product, precision=lax.Precision.HIGHEST)
            return jnp.transpose(rows_out.astype(jnp.bfloat16), (1, 0, 2)).reshape(
                piece_rows, hidden.shape[1], hidden.shape[2]
            )
        return run

    owned, branch_out = reduce_owned(
        grad_sum, block_owner, live_slots, dp_count, owner_cap, row_len,
        [branch_piece(i) for i in range(piece_count)],
        lambda parts: jnp.concatenate(parts, axis=0),
    )
    return (branch_out, owned[None])


def solution(mesh):
    placed = (
        P(("dp", "mp"), None),
        P(("dp", "mp"), None, None),
        P("mp", None, None),
        P("mp"),
        P("mp"),
        P("mp"),
        P("mp"),
    )
    return jax.shard_map(
        local,
        mesh=mesh,
        in_specs=placed,
        out_specs=(P("dp", None, "mp"), P("mp", "dp", None, None)),
        check_vma=False,
    )
```

```python
import jax
import jax.numpy as jnp
from jax import lax
from jax.sharding import PartitionSpec as P


def owner_ranks(block_owner, live_slots, dp_count):
    owner_hot = (
        (block_owner[:, None] == jnp.arange(dp_count, dtype=jnp.int32)[None, :])
        & live_slots[:, None]
    ).astype(jnp.int32)
    before = jnp.cumsum(owner_hot, axis=0) - owner_hot
    return jnp.sum(before * owner_hot, axis=1)


def slot_sources(targets, selected, slot_total):
    slot_ids = jnp.arange(slot_total, dtype=jnp.int32)
    chosen = selected[None, :] & (targets[None, :] == slot_ids[:, None])
    entry_ids = jnp.arange(targets.shape[0], dtype=jnp.int32)
    source_index = jnp.sum(jnp.where(chosen, entry_ids[None, :], 0), axis=1).astype(jnp.int32)
    return source_index, jnp.any(chosen, axis=1)


def local_part(table, keep, size_of_chunk):
    def part(c, h):
        rows = lax.dynamic_slice_in_dim(table, c * size_of_chunk, size_of_chunk, 0)
        half = rows.shape[1] // 2
        rows = rows[:, h * half:(h + 1) * half]
        if keep is None:
            return rows
        mask = lax.dynamic_slice_in_dim(keep, c * size_of_chunk, size_of_chunk, 0)
        return jnp.where(mask[:, None, None], rows, 0.0)
    return part


def reduce_owned(grad_sum, block_owner, live_slots, dp_count, owner_cap, row_len, pieces, join):
    x_count = dp_count // row_len
    half_cap = owner_cap // 2
    rank = owner_ranks(block_owner, live_slots, dp_count)
    owner_x = block_owner // row_len
    owner_z = block_owner % row_len
    half_slots = dp_count * half_cap
    in_a = live_slots & (rank < half_cap)
    in_b = live_slots & (rank >= half_cap)
    target_a = owner_z * (x_count * half_cap) + owner_x * half_cap + rank
    target_b = owner_x * (row_len * half_cap) + owner_z * half_cap + rank - half_cap
    source_a, keep_a = slot_sources(target_a, in_a, half_slots)
    source_b, keep_b = slot_sources(target_b, in_b, half_slots)
    tile = grad_sum.shape[1]
    table_a = jnp.take(grad_sum, source_a, axis=0, mode="clip")
    table_b = jnp.take(grad_sum, source_b, axis=0, mode="clip")

    dp_me = lax.axis_index("dp")
    me_z = dp_me % row_len
    me_x = dp_me // row_len

    def z_perm(shift):
        return [(i, (i // row_len) * row_len + (i % row_len + shift) % row_len) for i in range(dp_count)]

    def x_perm(shift):
        return [(i, (i + shift * row_len) % dp_count) for i in range(dp_count)]

    z_ring = (row_len, me_z, z_perm)
    x_ring = (x_count, me_x, x_perm)
    plan_a = [(z_ring, local_part(table_a, keep_a, x_count * half_cap)), (x_ring, None)]
    plan_b = [(x_ring, local_part(table_b, keep_b, row_len * half_cap)), (z_ring, None)]

    def start(ring, part):
        size, me, _ = ring
        return [part((me - 1) % size, 0), part((me + 1) % size, 1)]

    def finish(halves):
        return jnp.concatenate([halves[0], halves[1]], axis=1)

    def second_part(row_sum):
        def part(c, h):
            rows = lax.dynamic_slice_in_dim(row_sum, c * half_cap, half_cap, 0)
            return rows[:, h * (tile // 2):(h + 1) * (tile // 2)]
        return part

    rings = [plan_a, plan_b]
    states = []
    for plan in rings:
        (ring1, part1), _ = plan
        states.append({"stage": 0, "k": 0, "halves": start(ring1, part1), "part": part1})
    total_steps = max((p[0][0][0] - 1) + (p[1][0][0] - 1) for p in rings)
    tie_at = {max(1, (total_steps * (i + 1)) // (len(pieces) + 1)): i for i in range(len(pieces))}
    join_at = total_steps - 1
    results = [None] * len(pieces)
    for step in range(total_steps):
        received = []
        for plan, st in zip(rings, states):
            ring = plan[st["stage"]][0]
            received.append([
                lax.ppermute(st["halves"][0], "dp", ring[2](1)),
                lax.ppermute(st["halves"][1], "dp", ring[2](-1)),
            ])
        if step in tie_at:
            index = tie_at[step]
            received, results[index] = lax.optimization_barrier((received, pieces[index]()))
        if step == join_at:
            received, joined = lax.optimization_barrier((received, join(results)))
        for plan, st, got in zip(rings, states, received):
            size, me, _ = plan[st["stage"]][0]
            k = st["k"]
            part = st["part"]
            st["halves"] = [
                got[0] + part((me - k - 2) % size, 0),
                got[1] + part((me + k + 2) % size, 1),
            ]
            st["k"] = k + 1
            if st["k"] == size - 1 and st["stage"] == 0:
                row_sum = finish(st["halves"])
                ring2 = plan[1][0]
                st["stage"], st["k"] = 1, 0
                st["part"] = second_part(row_sum)
                st["halves"] = start(ring2, st["part"])
    if join_at <= max(tie_at):
        joined = join([part() if done is None else done for part, done in zip(pieces, results)])
    owned = jnp.concatenate([finish(states[0]["halves"]), finish(states[1]["halves"])], axis=0)
    return owned, joined


def gather_columns(upstream, mp_count):
    me = lax.axis_index("mp")
    width = upstream.shape[2] // mp_count
    pieces = [None] * mp_count
    for shift in range(mp_count):
        target = (me + shift) % mp_count
        piece = lax.dynamic_slice_in_dim(upstream, target * width, width, 2)
        if shift:
            perm = [(m, (m + shift) % mp_count) for m in range(mp_count)]
            piece = lax.ppermute(piece, "mp", perm)
        pieces[shift] = piece
    ordered = jnp.zeros((mp_count,) + pieces[0].shape, pieces[0].dtype)
    for shift in range(mp_count):
        ordered = lax.dynamic_update_index_in_dim(ordered, pieces[shift], (me - shift) % mp_count, 0)
    return ordered.reshape((mp_count * upstream.shape[0],) + upstream.shape[1:2] + (width,))


def local(tokens, upstream, deltas, block_row, block_column, block_owner, block_count):
    model_width = tokens.shape[1]
    tile_size = deltas.shape[1]
    slot_count = deltas.shape[0]
    mp_count = lax.axis_size("mp")
    dp_count = lax.axis_size("dp")
    hidden = gather_columns(upstream, mp_count)
    group_rows = hidden.shape[0]
    column_blocks = hidden.shape[1] * hidden.shape[2] // tile_size
    hidden_major = jnp.transpose(hidden.reshape(group_rows, column_blocks, tile_size), (1, 0, 2))
    upstream_chosen = jnp.take(hidden_major, block_column, axis=0, mode="clip")
    slot_ids = jnp.arange(slot_count, dtype=jnp.int32)
    live_slots = slot_ids < block_count[0]
    column_table = (
        live_slots[:, None]
        & (block_column[:, None] == jnp.arange(column_blocks, dtype=jnp.int32)[None, :])
    ).astype(jnp.float32)
    shard_rows = lax.all_gather(tokens, "mp", axis=0, tiled=True)
    row_count = shard_rows.shape[0]
    row_major = jnp.transpose(
        shard_rows.reshape(row_count, model_width // tile_size, tile_size), (1, 0, 2)
    )
    feature_tiles = jnp.take(row_major, block_row, axis=0, mode="clip")
    grad_sum = jnp.einsum(
        "kni,kno->kio", feature_tiles, upstream_chosen, preferred_element_type=jnp.float32
    )
    owner_cap = 3 * slot_count // (2 * dp_count)
    row_len = 8 if dp_count % 8 == 0 else dp_count
    piece_count = 4
    piece_rows = group_rows // piece_count

    def branch_piece(i):
        def run():
            rows_in = feature_tiles[:, i * piece_rows:(i + 1) * piece_rows]
            product = jnp.einsum("kni,kio->kno", rows_in, deltas, preferred_element_type=jnp.float32)
            rows_out = jnp.einsum("kc,kno->cno", column_table, product, precision=lax.Precision.HIGHEST)
            return jnp.transpose(rows_out.astype(jnp.bfloat16), (1, 0, 2)).reshape(
                piece_rows, hidden.shape[1], hidden.shape[2]
            )
        return run

    owned, branch_out = reduce_owned(
        grad_sum, block_owner, live_slots, dp_count, owner_cap, row_len,
        [branch_piece(i) for i in range(piece_count)],
        lambda parts: jnp.concatenate(parts, axis=0),
    )
    return (branch_out, owned[None])


def solution(mesh):
    placed = (
        P(("dp", "mp"), None),
        P(("dp", "mp"), None, None),
        P("mp", None, None),
        P("mp"),
        P("mp"),
        P("mp"),
        P("mp"),
    )
    return jax.shard_map(
        local,
        mesh=mesh,
        in_specs=placed,
        out_specs=(P("dp", None, "mp"), P("mp", "dp", None, None)),
        check_vma=False,
    )
```

```python
import jax
import jax.numpy as jnp
from jax import lax
from jax.sharding import PartitionSpec as P


def owner_ranks(block_owner, live_slots, dp_count):
    owner_hot = (
        (block_owner[:, None] == jnp.arange(dp_count, dtype=jnp.int32)[None, :])
        & live_slots[:, None]
    ).astype(jnp.int32)
    before = jnp.cumsum(owner_hot, axis=0) - owner_hot
    return jnp.sum(before * owner_hot, axis=1)


def slot_sources(targets, selected, slot_total):
    slot_ids = jnp.arange(slot_total, dtype=jnp.int32)
    chosen = selected[None, :] & (targets[None, :] == slot_ids[:, None])
    entry_ids = jnp.arange(targets.shape[0], dtype=jnp.int32)
    source_index = jnp.sum(jnp.where(chosen, entry_ids[None, :], 0), axis=1).astype(jnp.int32)
    return source_index, jnp.any(chosen, axis=1)


def local_part(table, keep, size_of_chunk):
    def part(c, h):
        rows = lax.dynamic_slice_in_dim(table, c * size_of_chunk, size_of_chunk, 0)
        half = rows.shape[1] // 2
        rows = rows[:, h * half:(h + 1) * half]
        if keep is None:
            return rows
        mask = lax.dynamic_slice_in_dim(keep, c * size_of_chunk, size_of_chunk, 0)
        return jnp.where(mask[:, None, None], rows, 0.0)
    return part


def reduce_owned(grad_sum, block_owner, live_slots, dp_count, owner_cap, row_len, pieces, join):
    x_count = dp_count // row_len
    half_cap = owner_cap // 2
    rank = owner_ranks(block_owner, live_slots, dp_count)
    owner_x = block_owner // row_len
    owner_z = block_owner % row_len
    half_slots = dp_count * half_cap
    in_a = live_slots & (rank < half_cap)
    in_b = live_slots & (rank >= half_cap)
    target_a = owner_z * (x_count * half_cap) + owner_x * half_cap + rank
    target_b = owner_x * (row_len * half_cap) + owner_z * half_cap + rank - half_cap
    source_a, keep_a = slot_sources(target_a, in_a, half_slots)
    source_b, keep_b = slot_sources(target_b, in_b, half_slots)
    tile = grad_sum.shape[1]
    table_a = jnp.take(grad_sum, source_a, axis=0, mode="clip")
    table_b = jnp.take(grad_sum, source_b, axis=0, mode="clip")

    dp_me = lax.axis_index("dp")
    me_z = dp_me % row_len
    me_x = dp_me // row_len

    def z_perm(shift):
        return [(i, (i // row_len) * row_len + (i % row_len + shift) % row_len) for i in range(dp_count)]

    def x_perm(shift):
        return [(i, (i + shift * row_len) % dp_count) for i in range(dp_count)]

    z_ring = (row_len, me_z, z_perm)
    x_ring = (x_count, me_x, x_perm)
    plan_a = [(z_ring, local_part(table_a, keep_a, x_count * half_cap)), (x_ring, None)]
    plan_b = [(x_ring, local_part(table_b, keep_b, row_len * half_cap)), (z_ring, None)]

    def start(ring, part):
        size, me, _ = ring
        return [part((me - 1) % size, 0), part((me + 1) % size, 1)]

    def finish(halves):
        return jnp.concatenate([halves[0], halves[1]], axis=1)

    def second_part(row_sum):
        def part(c, h):
            rows = lax.dynamic_slice_in_dim(row_sum, c * half_cap, half_cap, 0)
            return rows[:, h * (tile // 2):(h + 1) * (tile // 2)]
        return part

    rings = [plan_a, plan_b]
    states = []
    for plan in rings:
        (ring1, part1), _ = plan
        states.append({"stage": 0, "k": 0, "halves": start(ring1, part1), "part": part1})
    total_steps = max((p[0][0][0] - 1) + (p[1][0][0] - 1) for p in rings)
    tie_at = {max(1, (total_steps * (i + 1)) // (len(pieces) + 1)): i for i in range(len(pieces))}
    join_at = total_steps - 1
    tie_at = {(join_at if index == len(pieces) - 1 else step): index for step, index in tie_at.items()}
    results = [None] * len(pieces)
    for step in range(total_steps):
        received = []
        for plan, st in zip(rings, states):
            ring = plan[st["stage"]][0]
            received.append([
                lax.ppermute(st["halves"][0], "dp", ring[2](1)),
                lax.ppermute(st["halves"][1], "dp", ring[2](-1)),
            ])
        if step in tie_at:
            index = tie_at[step]
            received, results[index] = lax.optimization_barrier((received, pieces[index]()))
        if step == join_at:
            received, joined = lax.optimization_barrier((received, join(results)))
        for plan, st, got in zip(rings, states, received):
            size, me, _ = plan[st["stage"]][0]
            k = st["k"]
            part = st["part"]
            st["halves"] = [
                got[0] + part((me - k - 2) % size, 0),
                got[1] + part((me + k + 2) % size, 1),
            ]
            st["k"] = k + 1
            if st["k"] == size - 1 and st["stage"] == 0:
                row_sum = finish(st["halves"])
                ring2 = plan[1][0]
                st["stage"], st["k"] = 1, 0
                st["part"] = second_part(row_sum)
                st["halves"] = start(ring2, st["part"])
    if join_at >= total_steps:
        joined = join([part() if done is None else done for part, done in zip(pieces, results)])
    owned = jnp.concatenate([finish(states[0]["halves"]), finish(states[1]["halves"])], axis=0)
    return owned, joined


def gather_columns(upstream, mp_count):
    me = lax.axis_index("mp")
    width = upstream.shape[2] // mp_count
    pieces = [None] * mp_count
    for shift in range(mp_count):
        target = (me + shift) % mp_count
        piece = lax.dynamic_slice_in_dim(upstream, target * width, width, 2)
        if shift:
            perm = [(m, (m + shift) % mp_count) for m in range(mp_count)]
            piece = lax.ppermute(piece, "mp", perm)
        pieces[shift] = piece
    ordered = jnp.zeros((mp_count,) + pieces[0].shape, pieces[0].dtype)
    for shift in range(mp_count):
        ordered = lax.dynamic_update_index_in_dim(ordered, pieces[shift], (me - shift) % mp_count, 0)
    return ordered.reshape((mp_count * upstream.shape[0],) + upstream.shape[1:2] + (width,))


def local(tokens, upstream, deltas, block_row, block_column, block_owner, block_count):
    model_width = tokens.shape[1]
    tile_size = deltas.shape[1]
    slot_count = deltas.shape[0]
    mp_count = lax.axis_size("mp")
    dp_count = lax.axis_size("dp")
    hidden = gather_columns(upstream, mp_count)
    group_rows = hidden.shape[0]
    column_blocks = hidden.shape[1] * hidden.shape[2] // tile_size
    hidden_major = jnp.transpose(hidden.reshape(group_rows, column_blocks, tile_size), (1, 0, 2))
    upstream_chosen = jnp.take(hidden_major, block_column, axis=0, mode="clip")
    slot_ids = jnp.arange(slot_count, dtype=jnp.int32)
    live_slots = slot_ids < block_count[0]
    column_table = (
        live_slots[:, None]
        & (block_column[:, None] == jnp.arange(column_blocks, dtype=jnp.int32)[None, :])
    ).astype(jnp.float32)
    shard_rows = lax.all_gather(tokens, "mp", axis=0, tiled=True)
    row_count = shard_rows.shape[0]
    row_major = jnp.transpose(
        shard_rows.reshape(row_count, model_width // tile_size, tile_size), (1, 0, 2)
    )
    feature_tiles = jnp.take(row_major, block_row, axis=0, mode="clip")
    grad_sum = jnp.einsum(
        "kni,kno->kio", feature_tiles, upstream_chosen, preferred_element_type=jnp.float32
    )
    owner_cap = 3 * slot_count // (2 * dp_count)
    row_len = 8 if dp_count % 8 == 0 else dp_count
    piece_count = 4
    piece_rows = group_rows // piece_count

    def branch_piece(i):
        def run():
            rows_in = feature_tiles[:, i * piece_rows:(i + 1) * piece_rows]
            product = jnp.einsum("kni,kio->kno", rows_in, deltas, preferred_element_type=jnp.float32)
            rows_out = jnp.einsum("kc,kno->cno", column_table, product, precision=lax.Precision.HIGHEST)
            return jnp.transpose(rows_out.astype(jnp.bfloat16), (1, 0, 2)).reshape(
                piece_rows, hidden.shape[1], hidden.shape[2]
            )
        return run

    owned, branch_out = reduce_owned(
        grad_sum, block_owner, live_slots, dp_count, owner_cap, row_len,
        [branch_piece(i) for i in range(piece_count)],
        lambda parts: jnp.concatenate(parts, axis=0),
    )
    return (branch_out, owned[None])


def solution(mesh):
    placed = (
        P(("dp", "mp"), None),
        P(("dp", "mp"), None, None),
        P("mp", None, None),
        P("mp"),
        P("mp"),
        P("mp"),
        P("mp"),
    )
    return jax.shard_map(
        local,
        mesh=mesh,
        in_specs=placed,
        out_specs=(P("dp", None, "mp"), P("mp", "dp", None, None)),
        check_vma=False,
    )
```

```python
import jax
import jax.numpy as jnp
from jax import lax
from jax.sharding import PartitionSpec as P


def owner_ranks(block_owner, live_slots, dp_count):
    owner_hot = (
        (block_owner[:, None] == jnp.arange(dp_count, dtype=jnp.int32)[None, :])
        & live_slots[:, None]
    ).astype(jnp.int32)
    before = jnp.cumsum(owner_hot, axis=0) - owner_hot
    return jnp.sum(before * owner_hot, axis=1)


def slot_sources(targets, selected, slot_total):
    slot_ids = jnp.arange(slot_total, dtype=jnp.int32)
    chosen = selected[None, :] & (targets[None, :] == slot_ids[:, None])
    entry_ids = jnp.arange(targets.shape[0], dtype=jnp.int32)
    source_index = jnp.sum(jnp.where(chosen, entry_ids[None, :], 0), axis=1).astype(jnp.int32)
    return source_index, jnp.any(chosen, axis=1)


def local_part(table, keep, size_of_chunk):
    def part(c, h):
        rows = lax.dynamic_slice_in_dim(table, c * size_of_chunk, size_of_chunk, 0)
        half = rows.shape[1] // 2
        rows = rows[:, h * half:(h + 1) * half]
        if keep is None:
            return rows
        mask = lax.dynamic_slice_in_dim(keep, c * size_of_chunk, size_of_chunk, 0)
        return jnp.where(mask[:, None, None], rows, 0.0)
    return part


def reduce_owned(grad_sum, block_owner, live_slots, dp_count, owner_cap, row_len, pieces, join):
    x_count = dp_count // row_len
    half_cap = owner_cap // 2
    rank = owner_ranks(block_owner, live_slots, dp_count)
    owner_x = block_owner // row_len
    owner_z = block_owner % row_len
    half_slots = dp_count * half_cap
    in_a = live_slots & (rank < half_cap)
    in_b = live_slots & (rank >= half_cap)
    target_a = owner_z * (x_count * half_cap) + owner_x * half_cap + rank
    target_b = owner_x * (row_len * half_cap) + owner_z * half_cap + rank - half_cap
    source_a, keep_a = slot_sources(target_a, in_a, half_slots)
    source_b, keep_b = slot_sources(target_b, in_b, half_slots)
    tile = grad_sum.shape[1]
    table_a = jnp.take(grad_sum, source_a, axis=0, mode="clip")
    table_b = jnp.take(grad_sum, source_b, axis=0, mode="clip")

    dp_me = lax.axis_index("dp")
    me_z = dp_me % row_len
    me_x = dp_me // row_len

    def z_perm(shift):
        return [(i, (i // row_len) * row_len + (i % row_len + shift) % row_len) for i in range(dp_count)]

    def x_perm(shift):
        return [(i, (i + shift * row_len) % dp_count) for i in range(dp_count)]

    z_ring = (row_len, me_z, z_perm)
    x_ring = (x_count, me_x, x_perm)
    plan_a = [(z_ring, local_part(table_a, keep_a, x_count * half_cap)), (x_ring, None)]
    plan_b = [(x_ring, local_part(table_b, keep_b, row_len * half_cap)), (z_ring, None)]

    def start(ring, part):
        size, me, _ = ring
        return [part((me - 1) % size, 0), part((me + 1) % size, 1)]

    def finish(halves):
        return jnp.concatenate([halves[0], halves[1]], axis=1)

    def second_part(row_sum):
        def part(c, h):
            rows = lax.dynamic_slice_in_dim(row_sum, c * half_cap, half_cap, 0)
            return rows[:, h * (tile // 2):(h + 1) * (tile // 2)]
        return part

    rings = [plan_a, plan_b]
    states = []
    for plan in rings:
        (ring1, part1), _ = plan
        states.append({"stage": 0, "k": 0, "halves": start(ring1, part1), "part": part1})
    total_steps = max((p[0][0][0] - 1) + (p[1][0][0] - 1) for p in rings)
    tie_at = {1 + 2 * i: i for i in range(len(pieces))}
    join_at = total_steps - 1
    results = [None] * len(pieces)
    for step in range(total_steps):
        received = []
        for plan, st in zip(rings, states):
            ring = plan[st["stage"]][0]
            received.append([
                lax.ppermute(st["halves"][0], "dp", ring[2](1)),
                lax.ppermute(st["halves"][1], "dp", ring[2](-1)),
            ])
        if step in tie_at:
            index = tie_at[step]
            received, results[index] = lax.optimization_barrier((received, pieces[index]()))
        if step == join_at:
            received, joined = lax.optimization_barrier((received, join(results)))
        for plan, st, got in zip(rings, states, received):
            size, me, _ = plan[st["stage"]][0]
            k = st["k"]
            part = st["part"]
            st["halves"] = [
                got[0] + part((me - k - 2) % size, 0),
                got[1] + part((me + k + 2) % size, 1),
            ]
            st["k"] = k + 1
            if st["k"] == size - 1 and st["stage"] == 0:
                row_sum = finish(st["halves"])
                ring2 = plan[1][0]
                st["stage"], st["k"] = 1, 0
                st["part"] = second_part(row_sum)
                st["halves"] = start(ring2, st["part"])
    if join_at <= max(tie_at):
        joined = join([part() if done is None else done for part, done in zip(pieces, results)])
    owned = jnp.concatenate([finish(states[0]["halves"]), finish(states[1]["halves"])], axis=0)
    return owned, joined


def gather_columns(upstream, mp_count):
    me = lax.axis_index("mp")
    width = upstream.shape[2] // mp_count
    pieces = [None] * mp_count
    for shift in range(mp_count):
        target = (me + shift) % mp_count
        piece = lax.dynamic_slice_in_dim(upstream, target * width, width, 2)
        if shift:
            perm = [(m, (m + shift) % mp_count) for m in range(mp_count)]
            piece = lax.ppermute(piece, "mp", perm)
        pieces[shift] = piece
    ordered = jnp.zeros((mp_count,) + pieces[0].shape, pieces[0].dtype)
    for shift in range(mp_count):
        ordered = lax.dynamic_update_index_in_dim(ordered, pieces[shift], (me - shift) % mp_count, 0)
    return ordered.reshape((mp_count * upstream.shape[0],) + upstream.shape[1:2] + (width,))


def local(tokens, upstream, deltas, block_row, block_column, block_owner, block_count):
    model_width = tokens.shape[1]
    tile_size = deltas.shape[1]
    slot_count = deltas.shape[0]
    mp_count = lax.axis_size("mp")
    dp_count = lax.axis_size("dp")
    hidden = gather_columns(upstream, mp_count)
    group_rows = hidden.shape[0]
    column_blocks = hidden.shape[1] * hidden.shape[2] // tile_size
    hidden_major = jnp.transpose(hidden.reshape(group_rows, column_blocks, tile_size), (1, 0, 2))
    upstream_chosen = jnp.take(hidden_major, block_column, axis=0, mode="clip")
    slot_ids = jnp.arange(slot_count, dtype=jnp.int32)
    live_slots = slot_ids < block_count[0]
    column_table = (
        live_slots[:, None]
        & (block_column[:, None] == jnp.arange(column_blocks, dtype=jnp.int32)[None, :])
    ).astype(jnp.float32)
    shard_rows = lax.all_gather(tokens, "mp", axis=0, tiled=True)
    row_count = shard_rows.shape[0]
    row_major = jnp.transpose(
        shard_rows.reshape(row_count, model_width // tile_size, tile_size), (1, 0, 2)
    )
    feature_tiles = jnp.take(row_major, block_row, axis=0, mode="clip")
    grad_sum = jnp.einsum(
        "kni,kno->kio", feature_tiles, upstream_chosen, preferred_element_type=jnp.float32
    )
    owner_cap = 3 * slot_count // (2 * dp_count)
    row_len = 8 if dp_count % 8 == 0 else dp_count
    piece_count = 4
    piece_rows = group_rows // piece_count

    def branch_piece(i):
        def run():
            rows_in = feature_tiles[:, i * piece_rows:(i + 1) * piece_rows]
            product = jnp.einsum("kni,kio->kno", rows_in, deltas, preferred_element_type=jnp.float32)
            rows_out = jnp.einsum("kc,kno->cno", column_table, product, precision=lax.Precision.HIGHEST)
            return jnp.transpose(rows_out.astype(jnp.bfloat16), (1, 0, 2)).reshape(
                piece_rows, hidden.shape[1], hidden.shape[2]
            )
        return run

    owned, branch_out = reduce_owned(
        grad_sum, block_owner, live_slots, dp_count, owner_cap, row_len,
        [branch_piece(i) for i in range(piece_count)],
        lambda parts: jnp.concatenate(parts, axis=0),
    )
    return (branch_out, owned[None])


def solution(mesh):
    placed = (
        P(("dp", "mp"), None),
        P(("dp", "mp"), None, None),
        P("mp", None, None),
        P("mp"),
        P("mp"),
        P("mp"),
        P("mp"),
    )
    return jax.shard_map(
        local,
        mesh=mesh,
        in_specs=placed,
        out_specs=(P("dp", None, "mp"), P("mp", "dp", None, None)),
        check_vma=False,
    )
```

```python
import jax
import jax.numpy as jnp
from jax import lax
from jax.sharding import PartitionSpec as P


def owner_ranks(block_owner, live_slots, dp_count):
    owner_hot = (
        (block_owner[:, None] == jnp.arange(dp_count, dtype=jnp.int32)[None, :])
        & live_slots[:, None]
    ).astype(jnp.int32)
    before = jnp.cumsum(owner_hot, axis=0) - owner_hot
    return jnp.sum(before * owner_hot, axis=1)


def slot_sources(targets, selected, slot_total):
    slot_ids = jnp.arange(slot_total, dtype=jnp.int32)
    chosen = selected[None, :] & (targets[None, :] == slot_ids[:, None])
    entry_ids = jnp.arange(targets.shape[0], dtype=jnp.int32)
    source_index = jnp.sum(jnp.where(chosen, entry_ids[None, :], 0), axis=1).astype(jnp.int32)
    return source_index, jnp.any(chosen, axis=1)


def local_part(table, keep, size_of_chunk):
    def part(c, h):
        rows = lax.dynamic_slice_in_dim(table, c * size_of_chunk, size_of_chunk, 0)
        half = rows.shape[1] // 2
        rows = rows[:, h * half:(h + 1) * half]
        if keep is None:
            return rows
        mask = lax.dynamic_slice_in_dim(keep, c * size_of_chunk, size_of_chunk, 0)
        return jnp.where(mask[:, None, None], rows, 0.0)
    return part


def reduce_owned(grad_sum, block_owner, live_slots, dp_count, owner_cap, row_len, pieces, join):
    x_count = dp_count // row_len
    half_cap = owner_cap // 2
    rank = owner_ranks(block_owner, live_slots, dp_count)
    owner_x = block_owner // row_len
    owner_z = block_owner % row_len
    half_slots = dp_count * half_cap
    in_a = live_slots & (rank < half_cap)
    in_b = live_slots & (rank >= half_cap)
    target_a = owner_z * (x_count * half_cap) + owner_x * half_cap + rank
    target_b = owner_x * (row_len * half_cap) + owner_z * half_cap + rank - half_cap
    source_a, keep_a = slot_sources(target_a, in_a, half_slots)
    source_b, keep_b = slot_sources(target_b, in_b, half_slots)
    tile = grad_sum.shape[1]
    table_a = jnp.take(grad_sum, source_a, axis=0, mode="clip")
    table_b = jnp.take(grad_sum, source_b, axis=0, mode="clip")

    dp_me = lax.axis_index("dp")
    me_z = dp_me % row_len
    me_x = dp_me // row_len

    def z_perm(shift):
        return [(i, (i // row_len) * row_len + (i % row_len + shift) % row_len) for i in range(dp_count)]

    def x_perm(shift):
        return [(i, (i + shift * row_len) % dp_count) for i in range(dp_count)]

    z_ring = (row_len, me_z, z_perm)
    x_ring = (x_count, me_x, x_perm)
    plan_a = [(z_ring, local_part(table_a, keep_a, x_count * half_cap)), (x_ring, None)]
    plan_b = [(x_ring, local_part(table_b, keep_b, row_len * half_cap)), (z_ring, None)]

    def start(ring, part):
        size, me, _ = ring
        return [part((me - 1) % size, 0), part((me + 1) % size, 1)]

    def finish(halves):
        return jnp.concatenate([halves[0], halves[1]], axis=1)

    def second_part(row_sum):
        def part(c, h):
            rows = lax.dynamic_slice_in_dim(row_sum, c * half_cap, half_cap, 0)
            return rows[:, h * (tile // 2):(h + 1) * (tile // 2)]
        return part

    rings = [plan_a, plan_b]
    states = []
    for plan in rings:
        (ring1, part1), _ = plan
        states.append({"stage": 0, "k": 0, "halves": start(ring1, part1), "part": part1})
    total_steps = max((p[0][0][0] - 1) + (p[1][0][0] - 1) for p in rings)
    tie_at = {1 + 2 * i: i for i in range(len(pieces))}
    join_at = total_steps - 2
    results = [None] * len(pieces)
    for step in range(total_steps):
        received = []
        for plan, st in zip(rings, states):
            ring = plan[st["stage"]][0]
            received.append([
                lax.ppermute(st["halves"][0], "dp", ring[2](1)),
                lax.ppermute(st["halves"][1], "dp", ring[2](-1)),
            ])
        if step in tie_at:
            index = tie_at[step]
            received, results[index] = lax.optimization_barrier((received, pieces[index]()))
        if step == join_at:
            received, joined = lax.optimization_barrier((received, join(results)))
        for plan, st, got in zip(rings, states, received):
            size, me, _ = plan[st["stage"]][0]
            k = st["k"]
            part = st["part"]
            st["halves"] = [
                got[0] + part((me - k - 2) % size, 0),
                got[1] + part((me + k + 2) % size, 1),
            ]
            st["k"] = k + 1
            if st["k"] == size - 1 and st["stage"] == 0:
                row_sum = finish(st["halves"])
                ring2 = plan[1][0]
                st["stage"], st["k"] = 1, 0
                st["part"] = second_part(row_sum)
                st["halves"] = start(ring2, st["part"])
    if join_at <= max(tie_at):
        joined = join([part() if done is None else done for part, done in zip(pieces, results)])
    owned = jnp.concatenate([finish(states[0]["halves"]), finish(states[1]["halves"])], axis=0)
    return owned, joined


def gather_columns(upstream, mp_count):
    me = lax.axis_index("mp")
    width = upstream.shape[2] // mp_count
    pieces = [None] * mp_count
    for shift in range(mp_count):
        target = (me + shift) % mp_count
        piece = lax.dynamic_slice_in_dim(upstream, target * width, width, 2)
        if shift:
            perm = [(m, (m + shift) % mp_count) for m in range(mp_count)]
            piece = lax.ppermute(piece, "mp", perm)
        pieces[shift] = piece
    ordered = jnp.zeros((mp_count,) + pieces[0].shape, pieces[0].dtype)
    for shift in range(mp_count):
        ordered = lax.dynamic_update_index_in_dim(ordered, pieces[shift], (me - shift) % mp_count, 0)
    return ordered.reshape((mp_count * upstream.shape[0],) + upstream.shape[1:2] + (width,))


def local(tokens, upstream, deltas, block_row, block_column, block_owner, block_count):
    model_width = tokens.shape[1]
    tile_size = deltas.shape[1]
    slot_count = deltas.shape[0]
    mp_count = lax.axis_size("mp")
    dp_count = lax.axis_size("dp")
    hidden = gather_columns(upstream, mp_count)
    group_rows = hidden.shape[0]
    column_blocks = hidden.shape[1] * hidden.shape[2] // tile_size
    hidden_major = jnp.transpose(hidden.reshape(group_rows, column_blocks, tile_size), (1, 0, 2))
    upstream_chosen = jnp.take(hidden_major, block_column, axis=0, mode="clip")
    slot_ids = jnp.arange(slot_count, dtype=jnp.int32)
    live_slots = slot_ids < block_count[0]
    column_table = (
        live_slots[:, None]
        & (block_column[:, None] == jnp.arange(column_blocks, dtype=jnp.int32)[None, :])
    ).astype(jnp.float32)
    shard_rows = lax.all_gather(tokens, "mp", axis=0, tiled=True)
    row_count = shard_rows.shape[0]
    row_major = jnp.transpose(
        shard_rows.reshape(row_count, model_width // tile_size, tile_size), (1, 0, 2)
    )
    feature_tiles = jnp.take(row_major, block_row, axis=0, mode="clip")
    grad_sum = jnp.einsum(
        "kni,kno->kio", feature_tiles, upstream_chosen, preferred_element_type=jnp.float32
    )
    owner_cap = 3 * slot_count // (2 * dp_count)
    row_len = 8 if dp_count % 8 == 0 else dp_count
    piece_count = 4
    piece_rows = group_rows // piece_count

    def branch_piece(i):
        def run():
            rows_in = feature_tiles[:, i * piece_rows:(i + 1) * piece_rows]
            product = jnp.einsum("kni,kio->kno", rows_in, deltas, preferred_element_type=jnp.float32)
            rows_out = jnp.einsum("kc,kno->cno", column_table, product, precision=lax.Precision.HIGHEST)
            return jnp.transpose(rows_out.astype(jnp.bfloat16), (1, 0, 2)).reshape(
                piece_rows, hidden.shape[1], hidden.shape[2]
            )
        return run

    owned, branch_out = reduce_owned(
        grad_sum, block_owner, live_slots, dp_count, owner_cap, row_len,
        [branch_piece(i) for i in range(piece_count)],
        lambda parts: jnp.concatenate(parts, axis=0),
    )
    return (branch_out, owned[None])


def solution(mesh):
    placed = (
        P(("dp", "mp"), None),
        P(("dp", "mp"), None, None),
        P("mp", None, None),
        P("mp"),
        P("mp"),
        P("mp"),
        P("mp"),
    )
    return jax.shard_map(
        local,
        mesh=mesh,
        in_specs=placed,
        out_specs=(P("dp", None, "mp"), P("mp", "dp", None, None)),
        check_vma=False,
    )
```
